256 devices in a mesh: ep: 32 (over z, x), tp: 8 (over y, core).
Axes of the slice: x: 4, y: 4, z: 8, core: 2. Of those that a mesh axis runs over, the one named last changes fastest.
Arguments:
- tokens: bfloat16 [4096, 7168], P('ep', 'tp'), may hold values from -6 to 6
- cotangent: bfloat16 [4096, 7168], P('ep', 'tp'), may hold values from -6 to 6
- expert_ids: int32 [4096, 8], P('ep'), may hold values from 0 to 31, all different within a row; in each aligned block of 128 rows (0 to 127, 128 to 255, ...) at most 36 rows name the same one
- gate_values: float32 [4096, 8], P('ep'), may hold values from 0.02 to 0.5
- w_gate: bfloat16 [32, 7168, 1024], P('ep', 'tp'), may hold values from -0.0625 to 0.0625
- w_up: bfloat16 [32, 7168, 1024], P('ep', 'tp'), may hold values from -0.0625 to 0.0625
- w_down: bfloat16 [32, 1024, 7168], P('ep', None, 'tp'), may hold values from -0.1875 to 0.1875
Outputs:
- mixed: bfloat16 [4096, 7168], P('ep', 'tp')
- d_tokens: bfloat16 [4096, 7168], P('ep', 'tp')
- d_gates: float32 [4096, 8], P('ep')
The draws below stay inside these ranges and needn't reach their ends.
Inputs may be any that keep to these rules, and one draw needn't show every extreme that they name: `expert_ids`: each row names 8 different experts. Within each aligned block of 128 rows no expert is named by more than 36 rows, and in some block one expert is named by exactly 36 rows.
All inputs are finite; a program needn't handle non-finite values.
Results may differ from the reference program's by a relative error of at most 0.023.
Values may be sent and summed in bfloat16 or wider, within the bound.
No kernel may reach another device: no remote copies, remote signals or barrier semaphores. Data moves between devices by JAX's collectives and lax.ppermute only.
A program may use at most 64 MiB of HBM per device.

```python
import math
import jax
import jax.numpy as jnp
import numpy as np
from jax import lax

D = 7168
F = 1024
EXPERTS = 32
TOPK = 8
TOK_GRP = 128
CAP = 36
TOKENS = 4096
N_EP = 32
N_TP = 8


def block_scale(rng, dims, pieces, low, largest):
    def one(dim, shards_of):
        heights = jax.random.uniform(jax.random.fold_in(jax.random.fold_in(rng, 6), dim), (shards_of,), jnp.float32, low / len(pieces), largest / len(pieces))
        return jnp.repeat(jnp.exp(heights), dims[dim] // shards_of).reshape((-1,) + (1,) * (len(dims) - dim - 1))

    level = one(*pieces[0])
    for cut in pieces[1:]:
        level = level * one(*cut)
    return level


def deal_out(key, own, number, rows, amount, top, most, skew):
    ranking = jax.random.permutation(key, amount)
    crowded, common = load_shares(amount, rows * top, most, skew, True), load_shares(amount, rows * top, most, skew, False)
    places = jnp.arange(amount)

    def named(lengths, rotation):
        used = int((lengths > 0).sum())
        fixed = max(1, used // 4)
        moved = fixed + (places - fixed + rotation * (used - fixed)) % max(1, amount - fixed)
        return jnp.zeros((amount,), jnp.int32).at[ranking[jnp.where(places < fixed, places, moved)]].set(jnp.asarray(lengths, jnp.int32))

    lengths = jnp.where(number % 4 == 0, named(crowded, number // 4), named(common, number - number // 4 - 1))
    mixed = jax.random.permutation(jax.random.fold_in(own, 3), amount)
    giver, taker = mixed[0:amount // 2 * 2:2], mixed[1:amount // 2 * 2:2]
    margin = jnp.minimum(lengths[giver] - 1, most - lengths[taker]) // 2
    margin = jnp.where((giver == ranking[0]) | (taker == ranking[0]) | (lengths[taker] == 0), 0, jnp.maximum(margin, 0))
    moved = jax.random.randint(jax.random.fold_in(own, 4), (amount // 2,), 0, 1 << 20) % (margin + 1)
    lengths = lengths.at[giver].add(-moved).at[taker].add(moved)
    items = jnp.searchsorted(jnp.cumsum(lengths), jnp.arange(rows * top), side="right").astype(jnp.int32)
    table = items.reshape(top, rows).T
    table = table[jax.random.permutation(jax.random.fold_in(own, 1), rows)]
    rotation = jax.random.randint(jax.random.fold_in(own, 2), (rows, 1), 0, top)
    return jnp.take_along_axis(table, (jnp.arange(top)[None, :] + rotation) % top, axis=1)


def load_shares(count, total, limit, skew, full):
    loads = [(1 << 20) // math.isqrt(rank ** skew) + 1 for rank in range(1, count + 1)]
    largest = limit if full else min(limit, max(-(-total // count), total * loads[0] // sum(loads)))
    least = 1 if total - largest >= count - 1 else 0
    counts, rest = [largest] + [least] * (count - 1), total - largest - least * (count - 1)
    while rest > 0:
        movable = [i for i in range(1, count) if counts[i] < largest] or [i for i in range(1, count) if counts[i] < limit]
        pool, left = sum([loads[i] for i in movable]), rest
        for i in movable:
            addition = min(limit - counts[i], max(1, left * loads[i] // pool), rest)
            counts[i] = counts[i] + addition
            rest = rest - addition
    return np.array(counts)


def gaussian(own_key, extent, width, reach, shards=(), held_as=jnp.bfloat16):
    array = jax.random.normal(own_key, extent, jnp.float32) * width
    if len(shards) > 0:
        array = block_scale(own_key, extent, shards, -0.22, 0.18) * array
    return jnp.clip(array, min=-reach, max=reach).astype(held_as)


def setup_inputs(seed: int = 0) -> dict:
    splits = jax.random.split(jax.random.key(seed), 8)
    tokens = gaussian(splits[0], (TOKENS, D), 1.0, 6.0, ((0, 32), (1, 8)))
    cotangent = gaussian(splits[1], (TOKENS, D), 1.0, 6.0, ((0, 32), (1, 8)))
    expert_ids_keys = jax.random.split(jax.random.fold_in(splits[2], 1), TOKENS // TOK_GRP)
    expert_ids_turns = jax.random.permutation(jax.random.fold_in(splits[2], 3), TOKENS // TOK_GRP)
    expert_ids = jax.vmap(lambda own, number: deal_out(jax.random.fold_in(splits[2], 2), own, number, TOK_GRP, EXPERTS, TOPK, CAP, 1))(expert_ids_keys, expert_ids_turns).reshape((TOKENS, TOPK))
    gate_values = jnp.clip(jnp.exp(math.log(0.5) - 3.218876 * jax.random.uniform(splits[3], (TOKENS, TOPK), jnp.float32) ** block_scale(splits[3], (TOKENS, TOPK), ((0, 32),), -0.2, 0.2)), 0.02, 0.5)
    w_gate = gaussian(splits[4], (EXPERTS, D, F), D ** -0.5, 0.0625, ((0, 32), (1, 8)))
    w_up = gaussian(splits[5], (EXPERTS, D, F), D ** -0.5, 0.0625, ((0, 32), (1, 8)))
    w_down = gaussian(splits[6], (EXPERTS, F, D), F ** -0.5, 0.1875, ((0, 32), (2, 8)))
    return dict(tokens=tokens, cotangent=cotangent, expert_ids=expert_ids, gate_values=gate_values, w_gate=w_gate, w_up=w_up, w_down=w_down)


def split_dot(left, right):
    slice_width = D // N_TP
    total = jnp.zeros((left.shape[0], right.shape[1]), jnp.float32)
    for piece in range(N_TP):
        lower = piece * slice_width
        partial_sum = jnp.dot(left[:, lower:lower + slice_width], right[lower:lower + slice_width], preferred_element_type=jnp.float32)
        narrow = lax.optimization_barrier(partial_sum.astype(jnp.bfloat16))
        total = total + narrow.astype(jnp.float32)
    return total


def reference(tokens, cotangent, expert_ids, gate_values, w_gate, w_up, w_down):
    per_group = TOK_GRP * TOPK
    grouped = expert_ids.reshape(N_EP, per_group)
    onehot = (grouped[:, :, None] == jnp.arange(EXPERTS, dtype=jnp.int32)[None, None, :]).astype(jnp.int32)
    places = jnp.sum((jnp.cumsum(onehot, axis=1) - onehot) * onehot, axis=2).astype(jnp.int32)
    group_index = jnp.broadcast_to(jnp.arange(N_EP, dtype=jnp.int32)[:, None], (N_EP, per_group))
    slot_index = jnp.arange(N_EP * per_group, dtype=jnp.int32).reshape(N_EP, per_group)
    table = jnp.full((EXPERTS, N_EP, CAP), N_EP * per_group, dtype=jnp.int32)
    table = table.at[grouped, group_index, places].set(slot_index)
    gates_flat = gate_values.reshape(-1)

    def one_expert(carry, expert):
        mixed_acc, grad_acc, score_acc = carry
        slots = table[expert].reshape(-1)
        valid = slots < N_EP * per_group
        safe_slot = jnp.where(valid, slots, 0).astype(jnp.int32)
        token_row = (safe_slot // TOPK).astype(jnp.int32)
        rows = jnp.where(valid[:, None], tokens[token_row], jnp.zeros((), jnp.bfloat16))
        weights = jnp.where(valid, gates_flat[safe_slot], jnp.float32(0.0))
        grad_rows = jnp.where(valid[:, None], cotangent[token_row], jnp.zeros((), jnp.bfloat16))
        gate_in = split_dot(rows, w_gate[expert])
        up_in = split_dot(rows, w_up[expert])
        sigma = jax.nn.sigmoid(gate_in)
        hidden = (gate_in * sigma * up_in).astype(jnp.bfloat16)
        outputs = jnp.dot(hidden, w_down[expert], preferred_element_type=jnp.float32).astype(jnp.bfloat16)
        outputs_wide = outputs.astype(jnp.float32)
        target = jnp.where(valid, token_row, N_EP * TOK_GRP).astype(jnp.int32)
        mixed_acc = mixed_acc.at[target].add(weights[:, None] * outputs_wide, mode="drop")
        scores = jnp.sum(grad_rows.astype(jnp.float32) * outputs_wide, axis=1)
        score_target = jnp.where(valid, safe_slot, N_EP * per_group).astype(jnp.int32)
        score_acc = score_acc.at[score_target].add(scores, mode="drop")
        scaled = (weights[:, None] * grad_rows.astype(jnp.float32)).astype(jnp.bfloat16)
        d_hidden = split_dot(scaled, w_down[expert].T)
        d_gate_in = (d_hidden * up_in * sigma * (1.0 + gate_in * (1.0 - sigma))).astype(jnp.bfloat16)
        d_up_in = (d_hidden * gate_in * sigma).astype(jnp.bfloat16)
        d_slot = jnp.dot(d_gate_in, w_gate[expert].T, preferred_element_type=jnp.float32)
        d_slot = d_slot + jnp.dot(d_up_in, w_up[expert].T, preferred_element_type=jnp.float32)
        d_slot = d_slot.astype(jnp.bfloat16).astype(jnp.float32)
        grad_acc = grad_acc.at[target].add(d_slot, mode="drop")
        return (mixed_acc, grad_acc, score_acc), None

    start = (jnp.zeros((N_EP * TOK_GRP, D), jnp.float32), jnp.zeros((N_EP * TOK_GRP, D), jnp.float32), jnp.zeros((N_EP * per_group,), jnp.float32))
    (mixed_acc, grad_acc, score_acc), _ = lax.scan(one_expert, start, jnp.arange(EXPERTS, dtype=jnp.int32))
    return mixed_acc.astype(jnp.bfloat16), grad_acc.astype(jnp.bfloat16), score_acc.reshape(N_EP * TOK_GRP, TOPK)
```

```python
import jax
import jax.numpy as jnp
from jax import lax
from jax.sharding import PartitionSpec as P

CAP = 36
SLOTS = CAP


def slot_tables(expert_ids, experts):
    count, topk = expert_ids.shape
    onehot = (expert_ids[:, :, None] == jnp.arange(experts, dtype=jnp.int32)[None, None, :]).astype(
        jnp.float32
    )
    present = jnp.sum(onehot, axis=1)
    earlier = (jnp.arange(count)[:, None] > jnp.arange(count)[None, :]).astype(jnp.float32)
    before = jnp.dot(earlier, present, precision=lax.Precision.HIGHEST).astype(jnp.int32)
    places = jnp.sum(before[:, None, :] * onehot.astype(jnp.int32), axis=2)
    slot = expert_ids * SLOTS + places
    total = experts * SLOTS
    picks = slot.T[:, :, None] == jnp.arange(total, dtype=jnp.int32)[None, None, :]
    dispatch = jnp.any(picks, axis=0).T.astype(jnp.bfloat16)
    return (picks, dispatch)


def local(tokens, cotangent, expert_ids, gate_values, w_gate, w_up, w_down):
    groups = lax.axis_size("ep")
    holders = w_gate.shape[0]
    experts = groups * holders
    units = w_gate.shape[2]
    picks, dispatch = slot_tables(expert_ids, experts)
    send_tokens = jnp.dot(dispatch, tokens, preferred_element_type=jnp.float32).astype(jnp.bfloat16)
    cot_rows = jnp.dot(dispatch, cotangent, preferred_element_type=jnp.float32)
    slot_gate = jnp.sum(jnp.where(picks, gate_values.T[:, :, None], 0.0), axis=(0, 1))
    send_scaled = (slot_gate[:, None] * cot_rows).astype(jnp.bfloat16)

    arrived = lax.all_to_all(send_tokens, "ep", 0, 0, tiled=True)
    arrived_grad = lax.all_to_all(send_scaled, "ep", 0, 0, tiled=True)

    wg = w_gate[0]
    wu = w_up[0]
    wd = w_down[0]
    joined_part = jnp.concatenate(
        [
            jnp.dot(arrived, wg, preferred_element_type=jnp.float32),
            jnp.dot(arrived, wu, preferred_element_type=jnp.float32),
        ],
        axis=1,
    ).astype(jnp.bfloat16)
    joined = lax.psum_scatter(joined_part, "tp", scatter_dimension=0, tiled=True).astype(jnp.float32)
    gate_in = joined[:, :units]
    up_in = joined[:, units:]
    sigma = jax.nn.sigmoid(gate_in)
    hidden = (gate_in * sigma * up_in).astype(jnp.bfloat16)
    outputs = jnp.dot(
        lax.all_gather(hidden, "tp", axis=0, tiled=True), wd, preferred_element_type=jnp.float32
    ).astype(jnp.bfloat16)
    returned = lax.all_to_all(outputs, "ep", 0, 0, tiled=True)

    d_hidden_part = lax.dot_general(
        arrived_grad, wd, (((1,), (1,)), ((), ())), preferred_element_type=jnp.float32
    ).astype(jnp.bfloat16)
    d_hidden = lax.psum_scatter(d_hidden_part, "tp", scatter_dimension=0, tiled=True).astype(
        jnp.float32
    )
    d_gate_in = (d_hidden * up_in * sigma * (1.0 + gate_in * (1.0 - sigma))).astype(jnp.bfloat16)
    d_up_in = (d_hidden * gate_in * sigma).astype(jnp.bfloat16)
    piece = lax.all_gather(jnp.concatenate([d_gate_in, d_up_in], axis=1), "tp", axis=0, tiled=True)
    contract = (((1,), (1,)), ((), ()))
    slot_grads = (
        lax.dot_general(piece[:, :units], wg, contract, preferred_element_type=jnp.float32)
        + lax.dot_general(piece[:, units:], wu, contract, preferred_element_type=jnp.float32)
    ).astype(jnp.bfloat16)
    returned_grad = lax.all_to_all(slot_grads, "ep", 0, 0, tiled=True)

    gather = picks.astype(jnp.bfloat16)
    out_slots = jnp.einsum("kts,sd->ktd", gather, returned, preferred_element_type=jnp.float32)
    mixed = jnp.sum(gate_values.T[:, :, None] * out_slots, axis=0).astype(jnp.bfloat16)
    partial_scores = jnp.sum(cotangent[None, :, :].astype(jnp.float32) * out_slots, axis=2).T
    d_gates = lax.psum(partial_scores, "tp")
    d_tokens = jnp.einsum(
        "ts,sd->td", jnp.sum(gather, axis=0), returned_grad, preferred_element_type=jnp.float32
    ).astype(jnp.bfloat16)
    return (mixed, d_tokens, d_gates)


def solution(mesh):
    in_specs = (
        P("ep", "tp"),
        P("ep", "tp"),
        P("ep", None),
        P("ep", None),
        P("ep", "tp", None),
        P("ep", "tp", None),
        P("ep", None, "tp"),
    )
    out_specs = (P("ep", "tp"), P("ep", "tp"), P("ep", None))
    return jax.shard_map(local, mesh=mesh, in_specs=in_specs, out_specs=out_specs, check_vma=False)
```

```python
import jax
import jax.numpy as jnp
from jax import lax
from jax.sharding import PartitionSpec as P

CAP = 36
SLOTS = CAP


def slot_tables(expert_ids, experts):
    count, topk = expert_ids.shape
    onehot = (expert_ids[:, :, None] == jnp.arange(experts, dtype=jnp.int32)[None, None, :]).astype(
        jnp.float32
    )
    present = jnp.sum(onehot, axis=1)
    earlier = (jnp.arange(count)[:, None] > jnp.arange(count)[None, :]).astype(jnp.float32)
    before = jnp.dot(earlier, present, precision=lax.Precision.HIGHEST).astype(jnp.int32)
    places = jnp.sum(before[:, None, :] * onehot.astype(jnp.int32), axis=2)
    picks = (expert_ids.T[:, :, None, None] == jnp.arange(experts, dtype=jnp.int32)[None, None, :, None]) & (
        places.T[:, :, None, None] == jnp.arange(SLOTS, dtype=jnp.int32)[None, None, None, :]
    )
    dispatch = jnp.any(picks, axis=0).astype(jnp.bfloat16)
    return (picks, dispatch)


def local(tokens, cotangent, expert_ids, gate_values, w_gate, w_up, w_down):
    groups = lax.axis_size("ep")
    holders = w_gate.shape[0]
    experts = groups * holders
    units = w_gate.shape[2]
    picks, dispatch = slot_tables(expert_ids, experts)
    send_tokens = jnp.einsum(
        "tgc,td->gcd", dispatch, tokens, preferred_element_type=jnp.float32
    ).astype(jnp.bfloat16)
    cot_rows = jnp.einsum("tgc,td->gcd", dispatch, cotangent, preferred_element_type=jnp.float32)
    slot_gate = jnp.sum(jnp.where(picks, gate_values.T[:, :, None, None], 0.0), axis=(0, 1))
    send_scaled = (slot_gate[:, :, None] * cot_rows).astype(jnp.bfloat16)

    arrived = lax.all_to_all(send_tokens, "ep", 0, 0, tiled=True)

    w_both = jnp.concatenate([w_gate[0], w_up[0]], axis=1)
    wd = w_down[0]
    joined_part = jnp.einsum(
        "gcd,df->gcf", arrived, w_both, preferred_element_type=jnp.float32
    ).astype(jnp.bfloat16)
    send_scaled, joined_part = lax.optimization_barrier((send_scaled, joined_part))
    arrived_grad = lax.all_to_all(send_scaled, "ep", 0, 0, tiled=True)
    joined = lax.psum_scatter(joined_part, "tp", scatter_dimension=0, tiled=True)
    arrived_grad, joined = lax.optimization_barrier((arrived_grad, joined))
    joined = joined.astype(jnp.float32)
    gate_in = joined[:, :, :units]
    up_in = joined[:, :, units:]
    sigma = jax.nn.sigmoid(gate_in)
    hidden = (gate_in * sigma * up_in).astype(jnp.bfloat16)
    hidden_all = lax.all_gather(hidden, "tp", axis=0, tiled=True)
    outputs = jnp.einsum("gcf,fd->gcd", hidden_all, wd, preferred_element_type=jnp.float32).astype(
        jnp.bfloat16
    )
    arrived_grad, outputs = lax.optimization_barrier((arrived_grad, outputs))
    returned = lax.all_to_all(outputs, "ep", 0, 0, tiled=True)
    d_hidden_part = jnp.einsum(
        "gcd,fd->gcf", arrived_grad, wd, preferred_element_type=jnp.float32
    ).astype(jnp.bfloat16)
    d_hidden = lax.psum_scatter(d_hidden_part, "tp", scatter_dimension=0, tiled=True).astype(
        jnp.float32
    )
    d_gate_in = (d_hidden * up_in * sigma * (1.0 + gate_in * (1.0 - sigma))).astype(jnp.bfloat16)
    d_up_in = (d_hidden * gate_in * sigma).astype(jnp.bfloat16)
    piece = lax.all_gather(jnp.concatenate([d_gate_in, d_up_in], axis=2), "tp", axis=0, tiled=True)
    slot_grads = jnp.einsum(
        "gcf,df->gcd", piece, w_both, preferred_element_type=jnp.float32
    ).astype(jnp.bfloat16)
    returned_grad = lax.all_to_all(slot_grads, "ep", 0, 0, tiled=True)

    gather = picks.astype(jnp.bfloat16)
    out_slots = jnp.einsum("ktgc,gcd->ktd", gather, returned, preferred_element_type=jnp.float32)
    mixed = jnp.sum(gate_values.T[:, :, None] * out_slots, axis=0).astype(jnp.bfloat16)
    partial_scores = jnp.sum(cotangent[None, :, :].astype(jnp.float32) * out_slots, axis=2).T
    d_gates = lax.psum(partial_scores, "tp")
    d_tokens = jnp.einsum(
        "tgc,gcd->td", dispatch, returned_grad, preferred_element_type=jnp.float32
    ).astype(jnp.bfloat16)
    return (mixed, d_tokens, d_gates)


def solution(mesh):
    in_specs = (
        P("ep", "tp"),
        P("ep", "tp"),
        P("ep", None),
        P("ep", None),
        P("ep", "tp", None),
        P("ep", "tp", None),
        P("ep", None, "tp"),
    )
    out_specs = (P("ep", "tp"), P("ep", "tp"), P("ep", None))
    return jax.shard_map(local, mesh=mesh, in_specs=in_specs, out_specs=out_specs, check_vma=False)
```

```python
import jax
import jax.numpy as jnp
from jax import lax
from jax.sharding import PartitionSpec as P


CAP = 36
SLOTS = CAP


def slot_tables(expert_ids, experts):
    count, _ = expert_ids.shape
    onehot = (expert_ids[:, :, None] == jnp.arange(experts, dtype=jnp.int32)[None, None, :]).astype(
        jnp.float32
    )
    present = jnp.sum(onehot, axis=1)
    earlier = (jnp.arange(count)[:, None] > jnp.arange(count)[None, :]).astype(jnp.float32)
    before = jnp.dot(earlier, present, precision=lax.Precision.HIGHEST).astype(jnp.int32)
    places = jnp.sum(before[:, None, :] * onehot.astype(jnp.int32), axis=2)
    picks = (expert_ids.T[:, :, None, None] == jnp.arange(experts, dtype=jnp.int32)[None, None, :, None]) & (
        places.T[:, :, None, None] == jnp.arange(SLOTS, dtype=jnp.int32)[None, None, None, :]
    )
    dispatch = jnp.any(picks, axis=0).astype(jnp.bfloat16)
    return (picks, dispatch)


def body(tokens, cotangent, expert_ids, gate_values, w_gate, w_up, w_down):
    groups = lax.axis_size("ep")
    holders = w_gate.shape[0]
    experts = groups * holders
    units = w_gate.shape[2]
    picks, dispatch = slot_tables(expert_ids, experts)
    send_tokens = jnp.einsum(
        "tgc,td->gcd", dispatch, tokens, preferred_element_type=jnp.float32
    ).astype(jnp.bfloat16)
    cot_rows = jnp.einsum("tgc,td->gcd", dispatch, cotangent, preferred_element_type=jnp.float32)
    slot_gate = jnp.sum(jnp.where(picks, gate_values.T[:, :, None, None], 0.0), axis=(0, 1))
    send_scaled = (slot_gate[:, :, None] * cot_rows).astype(jnp.bfloat16)

    arrived = lax.all_to_all(send_tokens, "ep", 0, 0, tiled=True)

    w_both = jnp.concatenate([w_gate[0], w_up[0]], axis=1)
    wd = w_down[0]
    joined_part = jnp.einsum(
        "gcd,df->gcf", arrived, w_both, preferred_element_type=jnp.float32
    ).astype(jnp.bfloat16)
    send_scaled, joined_part = lax.optimization_barrier((send_scaled, joined_part))
    arrived_grad = lax.all_to_all(send_scaled, "ep", 0, 0, tiled=True)
    joined = lax.psum_scatter(joined_part, "tp", scatter_dimension=0, tiled=True)
    joined = joined.astype(jnp.float32)
    gate_in = joined[:, :, :units]
    up_in = joined[:, :, units:]
    sigma = jax.nn.sigmoid(gate_in)
    hidden = (gate_in * sigma * up_in).astype(jnp.bfloat16)
    hidden_all = lax.all_gather(hidden, "tp", axis=0, tiled=True)
    arrived_grad, hidden_all = lax.optimization_barrier((arrived_grad, hidden_all))
    outputs = jnp.einsum("gcf,fd->gcd", hidden_all, wd, preferred_element_type=jnp.float32).astype(
        jnp.bfloat16
    )
    returned = lax.all_to_all(outputs, "ep", 0, 0, tiled=True)
    d_hidden_part = jnp.einsum(
        "gcd,fd->gcf", arrived_grad, wd, preferred_element_type=jnp.float32
    ).astype(jnp.bfloat16)
    d_hidden = lax.psum_scatter(d_hidden_part, "tp", scatter_dimension=0, tiled=True).astype(
        jnp.float32
    )
    d_gate_in = (d_hidden * up_in * sigma * (1.0 + gate_in * (1.0 - sigma))).astype(jnp.bfloat16)
    d_up_in = (d_hidden * gate_in * sigma).astype(jnp.bfloat16)
    piece = lax.all_gather(jnp.concatenate([d_gate_in, d_up_in], axis=2), "tp", axis=0, tiled=True)
    slot_grads = jnp.einsum(
        "gcf,df->gcd", piece, w_both, preferred_element_type=jnp.float32
    ).astype(jnp.bfloat16)
    returned_grad = lax.all_to_all(slot_grads, "ep", 0, 0, tiled=True)

    gather = picks.astype(jnp.bfloat16)
    out_slots = jnp.einsum("ktgc,gcd->ktd", gather, returned, preferred_element_type=jnp.float32)
    mixed = jnp.sum(gate_values.T[:, :, None] * out_slots, axis=0).astype(jnp.bfloat16)
    partial_scores = jnp.sum(cotangent[None, :, :].astype(jnp.float32) * out_slots, axis=2).T
    d_gates = lax.psum(partial_scores, "tp")
    d_tokens = jnp.einsum(
        "tgc,gcd->td", dispatch, returned_grad, preferred_element_type=jnp.float32
    ).astype(jnp.bfloat16)
    return (mixed, d_tokens, d_gates)


def solution(mesh):
    in_specs = (
        P("ep", "tp"),
        P("ep", "tp"),
        P("ep", None),
        P("ep", None),
        P("ep", "tp", None),
        P("ep", "tp", None),
        P("ep", None, "tp"),
    )
    out_specs = (P("ep", "tp"), P("ep", "tp"), P("ep", None))
    return jax.shard_map(body, mesh=mesh, in_specs=in_specs, out_specs=out_specs, check_vma=False)
```

```python
import jax
import jax.numpy as jnp
from jax import lax
from jax.sharding import PartitionSpec as P


CAP = 36
SLOTS = CAP


def slot_tables(expert_ids, experts):
    count, _ = expert_ids.shape
    onehot = (expert_ids[:, :, None] == jnp.arange(experts, dtype=jnp.int32)[None, None, :]).astype(
        jnp.float32
    )
    present = jnp.sum(onehot, axis=1)
    earlier = (jnp.arange(count)[:, None] > jnp.arange(count)[None, :]).astype(jnp.float32)
    before = jnp.dot(earlier, present, precision=lax.Precision.HIGHEST).astype(jnp.int32)
    places = jnp.sum(before[:, None, :] * onehot.astype(jnp.int32), axis=2)
    picks = (expert_ids.T[:, :, None, None] == jnp.arange(experts, dtype=jnp.int32)[None, None, :, None]) & (
        places.T[:, :, None, None] == jnp.arange(SLOTS, dtype=jnp.int32)[None, None, None, :]
    )
    dispatch = jnp.any(picks, axis=0).astype(jnp.bfloat16)
    return (picks, dispatch)


def body(tokens, cotangent, expert_ids, gate_values, w_gate, w_up, w_down):
    groups = lax.axis_size("ep")
    holders = w_gate.shape[0]
    experts = groups * holders
    units = w_gate.shape[2]
    picks, dispatch = slot_tables(expert_ids, experts)
    send_tokens = jnp.einsum(
        "tgc,td->gcd", dispatch, tokens, preferred_element_type=jnp.float32
    ).astype(jnp.bfloat16)
    cot_rows = jnp.einsum("tgc,td->gcd", dispatch, cotangent, preferred_element_type=jnp.float32)
    slot_gate = jnp.sum(jnp.where(picks, gate_values.T[:, :, None, None], 0.0), axis=(0, 1))
    send_scaled = (slot_gate[:, :, None] * cot_rows).astype(jnp.bfloat16)

    arrived = lax.all_to_all(send_tokens, "ep", 0, 0, tiled=True)

    w_both = jnp.concatenate([w_gate[0], w_up[0]], axis=1)
    wd = w_down[0]
    joined_part = jnp.einsum(
        "gcd,df->gcf", arrived, w_both, preferred_element_type=jnp.float32
    ).astype(jnp.bfloat16)
    send_scaled, joined_part = lax.optimization_barrier((send_scaled, joined_part))
    arrived_grad = lax.all_to_all(send_scaled, "ep", 0, 0, tiled=True)
    joined = lax.psum_scatter(joined_part, "tp", scatter_dimension=0, tiled=True)
    joined = joined.astype(jnp.float32)
    gate_in = joined[:, :, :units]
    up_in = joined[:, :, units:]
    sigma = jax.nn.sigmoid(gate_in)
    hidden = (gate_in * sigma * up_in).astype(jnp.bfloat16)
    hidden_all = lax.all_gather(hidden, "tp", axis=0, tiled=True)
    outputs = jnp.einsum("gcf,fd->gcd", hidden_all, wd, preferred_element_type=jnp.float32).astype(
        jnp.bfloat16
    )
    returned = lax.all_to_all(outputs, "ep", 0, 0, tiled=True)
    d_hidden_part = jnp.einsum(
        "gcd,fd->gcf", arrived_grad, wd, preferred_element_type=jnp.float32
    ).astype(jnp.bfloat16)
    d_hidden = lax.psum_scatter(d_hidden_part, "tp", scatter_dimension=0, tiled=True).astype(
        jnp.float32
    )
    d_hidden, joined = lax.optimization_barrier((d_hidden, joined))
    gate_in = joined[:, :, :units]
    up_in = joined[:, :, units:]
    sigma = jax.nn.sigmoid(gate_in)
    d_gate_in = (d_hidden * up_in * sigma * (1.0 + gate_in * (1.0 - sigma))).astype(jnp.bfloat16)
    d_up_in = (d_hidden * gate_in * sigma).astype(jnp.bfloat16)
    piece = lax.all_gather(jnp.concatenate([d_gate_in, d_up_in], axis=2), "tp", axis=0, tiled=True)
    slot_grads = jnp.einsum(
        "gcf,df->gcd", piece, w_both, preferred_element_type=jnp.float32
    ).astype(jnp.bfloat16)
    returned_grad = lax.all_to_all(slot_grads, "ep", 0, 0, tiled=True)

    gather = picks.astype(jnp.bfloat16)
    out_slots = jnp.einsum("ktgc,gcd->ktd", gather, returned, preferred_element_type=jnp.float32)
    mixed = jnp.sum(gate_values.T[:, :, None] * out_slots, axis=0).astype(jnp.bfloat16)
    partial_scores = jnp.sum(cotangent[None, :, :].astype(jnp.float32) * out_slots, axis=2).T
    d_gates = lax.psum(partial_scores, "tp")
    d_tokens = jnp.einsum(
        "tgc,gcd->td", dispatch, returned_grad, preferred_element_type=jnp.float32
    ).astype(jnp.bfloat16)
    return (mixed, d_tokens, d_gates)


def solution(mesh):
    in_specs = (
        P("ep", "tp"),
        P("ep", "tp"),
        P("ep", None),
        P("ep", None),
        P("ep", "tp", None),
        P("ep", "tp", None),
        P("ep", None, "tp"),
    )
    out_specs = (P("ep", "tp"), P("ep", "tp"), P("ep", None))
    return jax.shard_map(body, mesh=mesh, in_specs=in_specs, out_specs=out_specs, check_vma=False)
```

```python
import jax
import jax.numpy as jnp
from jax import lax
from jax.sharding import PartitionSpec as P


CAP = 36
SLOTS = CAP


def slot_tables(expert_ids, experts):
    count, _ = expert_ids.shape
    onehot = (expert_ids[:, :, None] == jnp.arange(experts, dtype=jnp.int32)[None, None, :]).astype(
        jnp.float32
    )
    present = jnp.sum(onehot, axis=1)
    earlier = (jnp.arange(count)[:, None] > jnp.arange(count)[None, :]).astype(jnp.float32)
    before = jnp.dot(earlier, present, precision=lax.Precision.HIGHEST).astype(jnp.int32)
    places = jnp.sum(before[:, None, :] * onehot.astype(jnp.int32), axis=2)
    picks = (expert_ids.T[:, :, None, None] == jnp.arange(experts, dtype=jnp.int32)[None, None, :, None]) & (
        places.T[:, :, None, None] == jnp.arange(SLOTS, dtype=jnp.int32)[None, None, None, :]
    )
    dispatch = jnp.any(picks, axis=0).astype(jnp.bfloat16)
    return (picks, dispatch)


def body(tokens, cotangent, expert_ids, gate_values, w_gate, w_up, w_down):
    groups = lax.axis_size("ep")
    holders = w_gate.shape[0]
    experts = groups * holders
    units = w_gate.shape[2]
    picks, dispatch = slot_tables(expert_ids, experts)
    send_tokens = jnp.einsum(
        "tgc,td->gcd", dispatch, tokens, preferred_element_type=jnp.float32
    ).astype(jnp.bfloat16)
    cot_rows = jnp.einsum("tgc,td->gcd", dispatch, cotangent, preferred_element_type=jnp.float32)
    slot_gate = jnp.sum(jnp.where(picks, gate_values.T[:, :, None, None], 0.0), axis=(0, 1))
    send_scaled = (slot_gate[:, :, None] * cot_rows).astype(jnp.bfloat16)

    arrived = lax.all_to_all(send_tokens, "ep", 0, 0, tiled=True)

    w_both = jnp.concatenate([w_gate[0], w_up[0]], axis=1)
    wd = w_down[0]
    joined_part = jnp.einsum(
        "gcd,df->gcf", arrived, w_both, preferred_element_type=jnp.float32
    ).astype(jnp.bfloat16)
    send_scaled, joined_part = lax.optimization_barrier((send_scaled, joined_part))
    arrived_grad = lax.all_to_all(send_scaled, "ep", 0, 0, tiled=True)
    joined = lax.psum_scatter(joined_part, "tp", scatter_dimension=0, tiled=True)
    joined = joined.astype(jnp.float32)
    gate_in = joined[:, :, :units]
    up_in = joined[:, :, units:]
    sigma = jax.nn.sigmoid(gate_in)
    hidden = (gate_in * sigma * up_in).astype(jnp.bfloat16)
    hidden_all = lax.all_gather(hidden, "tp", axis=0, tiled=True)
    outputs = jnp.einsum("gcf,fd->gcd", hidden_all, wd, preferred_element_type=jnp.float32).astype(
        jnp.bfloat16
    )
    returned = lax.all_to_all(outputs, "ep", 0, 0, tiled=True)
    d_hidden_part = jnp.einsum(
        "gcd,fd->gcf", arrived_grad, wd, preferred_element_type=jnp.float32
    ).astype(jnp.bfloat16)
    d_hidden = lax.psum_scatter(d_hidden_part, "tp", scatter_dimension=0, tiled=True).astype(
        jnp.float32
    )
    d_hidden, joined = lax.optimization_barrier((d_hidden, joined))
    gate_in = joined[:, :, :units]
    up_in = joined[:, :, units:]
    sigma = jax.nn.sigmoid(gate_in)
    d_gate_in = (d_hidden * up_in * sigma * (1.0 + gate_in * (1.0 - sigma))).astype(jnp.bfloat16)
    d_up_in = (d_hidden * gate_in * sigma).astype(jnp.bfloat16)
    gate_all = lax.all_gather(d_gate_in, "tp", axis=0, tiled=True)
    up_all = lax.all_gather(d_up_in, "tp", axis=0, tiled=True)
    slot_grads = (
        jnp.einsum("gcf,df->gcd", gate_all, w_gate[0], preferred_element_type=jnp.float32)
        + jnp.einsum("gcf,df->gcd", up_all, w_up[0], preferred_element_type=jnp.float32)
    ).astype(jnp.bfloat16)
    returned_grad = lax.all_to_all(slot_grads, "ep", 0, 0, tiled=True)

    gather = picks.astype(jnp.bfloat16)
    out_slots = jnp.einsum("ktgc,gcd->ktd", gather, returned, preferred_element_type=jnp.float32)
    mixed = jnp.sum(gate_values.T[:, :, None] * out_slots, axis=0).astype(jnp.bfloat16)
    partial_scores = jnp.sum(cotangent[None, :, :].astype(jnp.float32) * out_slots, axis=2).T
    d_gates = lax.psum(partial_scores, "tp")
    d_tokens = jnp.einsum(
        "tgc,gcd->td", dispatch, returned_grad, preferred_element_type=jnp.float32
    ).astype(jnp.bfloat16)
    return (mixed, d_tokens, d_gates)


def solution(mesh):
    in_specs = (
        P("ep", "tp"),
        P("ep", "tp"),
        P("ep", None),
        P("ep", None),
        P("ep", "tp", None),
        P("ep", "tp", None),
        P("ep", None, "tp"),
    )
    out_specs = (P("ep", "tp"), P("ep", "tp"), P("ep", None))
    return jax.shard_map(body, mesh=mesh, in_specs=in_specs, out_specs=out_specs, check_vma=False)
```

```python
import jax
import jax.numpy as jnp
from jax import lax
from jax.sharding import PartitionSpec as P


CAP = 36
SLOTS = CAP


def slot_tables(expert_ids, experts):
    count, _ = expert_ids.shape
    onehot = (expert_ids[:, :, None] == jnp.arange(experts, dtype=jnp.int32)[None, None, :]).astype(
        jnp.float32
    )
    present = jnp.sum(onehot, axis=1)
    earlier = (jnp.arange(count)[:, None] > jnp.arange(count)[None, :]).astype(jnp.float32)
    before = jnp.dot(earlier, present, precision=lax.Precision.HIGHEST).astype(jnp.int32)
    places = jnp.sum(before[:, None, :] * onehot.astype(jnp.int32), axis=2)
    picks = (expert_ids.T[:, :, None, None] == jnp.arange(experts, dtype=jnp.int32)[None, None, :, None]) & (
        places.T[:, :, None, None] == jnp.arange(SLOTS, dtype=jnp.int32)[None, None, None, :]
    )
    dispatch = jnp.any(picks, axis=0).astype(jnp.bfloat16)
    return (picks, dispatch)


def body(tokens, cotangent, expert_ids, gate_values, w_gate, w_up, w_down):
    groups = lax.axis_size("ep")
    holders = w_gate.shape[0]
    experts = groups * holders
    units = w_gate.shape[2]
    picks, dispatch = slot_tables(expert_ids, experts)
    send_tokens = jnp.einsum(
        "tgc,td->gcd", dispatch, tokens, preferred_element_type=jnp.float32
    ).astype(jnp.bfloat16)
    cot_rows = jnp.einsum("tgc,td->gcd", dispatch, cotangent, preferred_element_type=jnp.float32)
    slot_gate = jnp.sum(jnp.where(picks, gate_values.T[:, :, None, None], 0.0), axis=(0, 1))
    send_scaled = (slot_gate[:, :, None] * cot_rows).astype(jnp.bfloat16)

    arrived = lax.all_to_all(send_tokens, "ep", 0, 0, tiled=True)

    w_both = jnp.concatenate([w_gate[0], w_up[0]], axis=1)
    wd = w_down[0]
    joined_part = jnp.einsum(
        "gcd,df->gcf", arrived, w_both, preferred_element_type=jnp.float32
    ).astype(jnp.bfloat16)
    send_scaled, joined_part = lax.optimization_barrier((send_scaled, joined_part))
    arrived_grad = lax.all_to_all(send_scaled, "ep", 0, 0, tiled=True)
    joined = lax.psum_scatter(joined_part, "tp", scatter_dimension=0, tiled=True)
    joined = joined.astype(jnp.float32)
    gate_in = joined[:, :, :units]
    up_in = joined[:, :, units:]
    sigma = jax.nn.sigmoid(gate_in)
    hidden = (gate_in * sigma * up_in).astype(jnp.bfloat16)
    hidden_all = lax.all_gather(hidden, "tp", axis=0, tiled=True)
    outputs = jnp.einsum("gcf,fd->gcd", hidden_all, wd, preferred_element_type=jnp.float32).astype(
        jnp.bfloat16
    )
    returned = lax.all_to_all(outputs, "ep", 0, 0, tiled=True)
    d_hidden_part = jnp.einsum(
        "gcd,fd->gcf", arrived_grad, wd, preferred_element_type=jnp.float32
    ).astype(jnp.bfloat16)
    ranks = lax.axis_size("tp")
    spread = lax.all_to_all(d_hidden_part, "tp", 0, 0, tiled=True)
    d_hidden = jnp.sum(
        spread.reshape((ranks, -1) + spread.shape[1:]).astype(jnp.float32), axis=0
    )
    d_hidden, joined = lax.optimization_barrier((d_hidden, joined))
    gate_in = joined[:, :, :units]
    up_in = joined[:, :, units:]
    sigma = jax.nn.sigmoid(gate_in)
    d_gate_in = (d_hidden * up_in * sigma * (1.0 + gate_in * (1.0 - sigma))).astype(jnp.bfloat16)
    d_up_in = (d_hidden * gate_in * sigma).astype(jnp.bfloat16)
    piece = lax.all_gather(jnp.concatenate([d_gate_in, d_up_in], axis=2), "tp", axis=0, tiled=True)
    slot_grads = jnp.einsum(
        "gcf,df->gcd", piece, w_both, preferred_element_type=jnp.float32
    ).astype(jnp.bfloat16)
    returned_grad = lax.all_to_all(slot_grads, "ep", 0, 0, tiled=True)

    gather = picks.astype(jnp.bfloat16)
    out_slots = jnp.einsum("ktgc,gcd->ktd", gather, returned, preferred_element_type=jnp.float32)
    mixed = jnp.sum(gate_values.T[:, :, None] * out_slots, axis=0).astype(jnp.bfloat16)
    partial_scores = jnp.sum(cotangent[None, :, :].astype(jnp.float32) * out_slots, axis=2).T
    d_gates = lax.psum(partial_scores, "tp")
    d_tokens = jnp.einsum(
        "tgc,gcd->td", dispatch, returned_grad, preferred_element_type=jnp.float32
    ).astype(jnp.bfloat16)
    return (mixed, d_tokens, d_gates)


def solution(mesh):
    in_specs = (
        P("ep", "tp"),
        P("ep", "tp"),
        P("ep", None),
        P("ep", None),
        P("ep", "tp", None),
        P("ep", "tp", None),
        P("ep", None, "tp"),
    )
    out_specs = (P("ep", "tp"), P("ep", "tp"), P("ep", None))
    return jax.shard_map(body, mesh=mesh, in_specs=in_specs, out_specs=out_specs, check_vma=False)
```

```python
import jax
import jax.numpy as jnp
from jax import lax
from jax.sharding import PartitionSpec as P


CAP = 36
SLOTS = CAP


def slot_tables(expert_ids, experts):
    count, _ = expert_ids.shape
    onehot = (expert_ids[:, :, None] == jnp.arange(experts, dtype=jnp.int32)[None, None, :]).astype(
        jnp.float32
    )
    present = jnp.sum(onehot, axis=1)
    earlier = (jnp.arange(count)[:, None] > jnp.arange(count)[None, :]).astype(jnp.float32)
    before = jnp.dot(earlier, present, precision=lax.Precision.HIGHEST).astype(jnp.int32)
    places = jnp.sum(before[:, None, :] * onehot.astype(jnp.int32), axis=2)
    picks = (expert_ids.T[:, :, None, None] == jnp.arange(experts, dtype=jnp.int32)[None, None, :, None]) & (
        places.T[:, :, None, None] == jnp.arange(SLOTS, dtype=jnp.int32)[None, None, None, :]
    )
    chosen = (expert_ids[None, None, :, :] == jnp.arange(experts, dtype=jnp.int32)[:, None, None, None]) & (
        places[None, None, :, :] == jnp.arange(SLOTS, dtype=jnp.int32)[None, :, None, None]
    )
    dispatch = jnp.any(chosen, axis=3).astype(jnp.bfloat16)
    return (picks, dispatch)


def body(tokens, cotangent, expert_ids, gate_values, w_gate, w_up, w_down):
    groups = lax.axis_size("ep")
    holders = w_gate.shape[0]
    experts = groups * holders
    units = w_gate.shape[2]
    picks, dispatch = slot_tables(expert_ids, experts)
    send_tokens = jnp.einsum(
        "gct,td->gcd", dispatch, tokens, preferred_element_type=jnp.float32
    ).astype(jnp.bfloat16)
    cot_rows = jnp.einsum("gct,td->gcd", dispatch, cotangent, preferred_element_type=jnp.float32)
    slot_gate = jnp.sum(jnp.where(picks, gate_values.T[:, :, None, None], 0.0), axis=(0, 1))
    send_scaled = (slot_gate[:, :, None] * cot_rows).astype(jnp.bfloat16)

    arrived = lax.all_to_all(send_tokens, "ep", 0, 0, tiled=True)

    w_both = jnp.concatenate([w_gate[0], w_up[0]], axis=1)
    wd = w_down[0]
    joined_part = jnp.einsum(
        "gcd,df->gcf", arrived, w_both, preferred_element_type=jnp.float32
    ).astype(jnp.bfloat16)
    send_scaled, joined_part = lax.optimization_barrier((send_scaled, joined_part))
    arrived_grad = lax.all_to_all(send_scaled, "ep", 0, 0, tiled=True)
    joined = lax.psum_scatter(joined_part, "tp", scatter_dimension=0, tiled=True)
    joined = joined.astype(jnp.float32)
    gate_in = joined[:, :, :units]
    up_in = joined[:, :, units:]
    sigma = jax.nn.sigmoid(gate_in)
    hidden = (gate_in * sigma * up_in).astype(jnp.bfloat16)
    hidden_all = lax.all_gather(hidden, "tp", axis=0, tiled=True)
    outputs = jnp.einsum("gcf,fd->gcd", hidden_all, wd, preferred_element_type=jnp.float32).astype(
        jnp.bfloat16
    )
    returned = lax.all_to_all(outputs, "ep", 0, 0, tiled=True)
    d_hidden_part = jnp.einsum("gcd,fd->gcf", arrived_grad, wd, preferred_element_type=jnp.float32).astype(jnp.bfloat16)
    d_hidden = lax.psum_scatter(d_hidden_part, "tp", scatter_dimension=0, tiled=True).astype(
        jnp.float32
    )
    d_hidden, joined = lax.optimization_barrier((d_hidden, joined))
    gate_in = joined[:, :, :units]
    up_in = joined[:, :, units:]
    sigma = jax.nn.sigmoid(gate_in)
    d_gate_in = (d_hidden * up_in * sigma * (1.0 + gate_in * (1.0 - sigma))).astype(jnp.bfloat16)
    d_up_in = (d_hidden * gate_in * sigma).astype(jnp.bfloat16)
    piece = lax.all_gather(jnp.concatenate([d_gate_in, d_up_in], axis=2), "tp", axis=0, tiled=True)
    slot_grads = jnp.einsum(
        "gcf,df->gcd", piece, w_both, preferred_element_type=jnp.float32
    ).astype(jnp.bfloat16)
    returned_grad = lax.all_to_all(slot_grads, "ep", 0, 0, tiled=True)

    gather = picks.astype(jnp.bfloat16)
    out_slots = jnp.einsum("ktgc,gcd->ktd", gather, returned, preferred_element_type=jnp.float32)
    mixed = jnp.sum(gate_values.T[:, :, None] * out_slots, axis=0).astype(jnp.bfloat16)
    partial_scores = jnp.sum(cotangent[None, :, :].astype(jnp.float32) * out_slots, axis=2).T
    d_gates = lax.psum(partial_scores, "tp")
    d_tokens = jnp.einsum(
        "gct,gcd->td", dispatch, returned_grad, preferred_element_type=jnp.float32
    ).astype(jnp.bfloat16)
    return (mixed, d_tokens, d_gates)


def solution(mesh):
    in_specs = (
        P("ep", "tp"),
        P("ep", "tp"),
        P("ep", None),
        P("ep", None),
        P("ep", "tp", None),
        P("ep", "tp", None),
        P("ep", None, "tp"),
    )
    out_specs = (P("ep", "tp"), P("ep", "tp"), P("ep", None))
    return jax.shard_map(body, mesh=mesh, in_specs=in_specs, out_specs=out_specs, check_vma=False)
```
